512 devices in a mesh: expert: 32 (over y, z_hi, x), dp: 16 (over z_lo, core).
Axes of the slice: x: 4, y: 4, z: 16 (z_hi: 2, z_lo: 8; z = z_hi * 8 + z_lo), core: 2. Of those that a mesh axis runs over, the one named last changes fastest.
Arguments:
- tokens: bfloat16 [4096, 3584], P('expert'), may hold values from -6 to 6
- expert_ids: int32 [4096, 8], P('expert'), may hold values from 0 to 31, all different within a row; in each aligned block of 128 rows (0 to 127, 128 to 255, ...) at most 48 rows name the same one
- route_weights: float32 [4096, 8], P('expert'), may hold values from 0.05 to 0.45
- gate_up_panels: bfloat16 [32, 16, 1792, 256], P('expert', 'dp'), may hold values from -0.09375 to 0.09375
- down_panels: bfloat16 [32, 1024, 3584], P('expert', None, 'dp'), may hold values from -0.1875 to 0.1875
- partner: int32 [32], replicated, may hold values from 0 to 31, as said below
Outputs:
- moe_out: bfloat16 [4096, 3584], P('expert', 'dp')
- new_gate_up: bfloat16 [32, 16, 1792, 256], P('expert', 'dp')
- new_down: bfloat16 [32, 1024, 3584], P('expert', None, 'dp')
The draws below stay inside these ranges and needn't reach their ends.
Inputs may be any that keep to these rules, and one draw needn't show every extreme that they name: `expert_ids`: in the 128 rows of one index of the expert axis, each row names 8 different experts and no expert is named by more than 48 rows. partner[i] is i, i XOR 1 or i XOR 2, the same of these for the four indices of each aligned group of four; partner[partner[i]] = i; some group takes XOR 1 and some group XOR 2.
All inputs are finite; a program needn't handle non-finite values.
Results may differ from the reference program's by a relative error of at most 0.0057.
Values may be sent and summed in bfloat16 or wider, within the bound.
No kernel may reach another device: no remote copies, remote signals or barrier semaphores. Data moves between devices by JAX's collectives and lax.ppermute only.
A program may use at most 64 MiB of HBM per device.

```python
import math
import jax
import jax.numpy as jnp
import numpy as np
from jax import lax

D = 3584
FF = 1024
TOP = 8
TOK = 128
EXPERTS = 32
TOKENS = 4096
CAP = 48
HID = 128
N_EXPERT = 32
N_DP = 16


def draw_partner(key, part):
    group_count = EXPERTS // 4
    first_key, second_key = jax.random.split(jax.random.fold_in(key, 17))
    kinds = jax.random.randint(first_key, (group_count,), 0, 3)
    order = jax.random.permutation(second_key, group_count)
    kinds = kinds.at[order[0]].set(0).at[order[1]].set(1)
    masks = jnp.array([1, 2, 0], dtype=jnp.int32)[kinds]
    indices = jnp.arange(EXPERTS, dtype=jnp.int32)
    return jnp.bitwise_xor(indices, jnp.repeat(masks, 4)).astype(jnp.int32)


def level_of(rng, dims, pieces, smallest, largest):
    gain, own = 1.0, jax.random.fold_in(rng, 6)
    for axis_at, shards_of in pieces:
        heights = jnp.exp(jax.random.uniform(jax.random.fold_in(own, axis_at), (shards_of,), jnp.float32, smallest / len(pieces), largest / len(pieces)))
        gain = gain * jnp.repeat(heights, dims[axis_at] // shards_of).reshape([-1 if axis == axis_at else 1 for axis in range(len(dims))])
    return gain


def deal_out(stream_key, own, number, rows, count, top, most, slope):
    ranking = jax.random.permutation(stream_key, count)
    heavy_load, ordinary = shares(count, rows * top, most, slope, True), shares(count, rows * top, most, slope, False)
    places = jnp.arange(count)

    def named(sizes, offset_by):
        used = int((sizes > 0).sum())
        fixed = max(1, used // 4)
        passed = fixed + (places - fixed + offset_by * (used - fixed)) % max(1, count - fixed)
        return jnp.zeros((count,), jnp.int32).at[ranking[jnp.where(places < fixed, places, passed)]].set(jnp.asarray(sizes, jnp.int32))

    sizes = jnp.where(number % 4 == 0, named(heavy_load, number // 4), named(ordinary, number - number // 4 - 1))
    mixed = jax.random.permutation(jax.random.fold_in(own, 3), count)
    giver, sink = mixed[0:count // 2 * 2:2], mixed[1:count // 2 * 2:2]
    room = jnp.minimum(sizes[giver] - 1, most - sizes[sink]) // 2
    room = jnp.where((giver == ranking[0]) | (sink == ranking[0]) | (sizes[sink] == 0), 0, jnp.maximum(room, 0))
    passed = jax.random.randint(jax.random.fold_in(own, 4), (count // 2,), 0, 1 << 20) % (room + 1)
    sizes = sizes.at[giver].add(-passed).at[sink].add(passed)
    members = jnp.searchsorted(jnp.cumsum(sizes), jnp.arange(rows * top), side="right").astype(jnp.int32)
    listing = members.reshape(top, rows).T
    listing = listing[jax.random.permutation(jax.random.fold_in(own, 1), rows)]
    offset_by = jax.random.randint(jax.random.fold_in(own, 2), (rows, 1), 0, top)
    return jnp.take_along_axis(listing, (jnp.arange(top)[None, :] + offset_by) % top, axis=1)


def shares(count, total, limit, skew, full):
    portions = [(1 << 20) // math.isqrt(rank ** skew) + 1 for rank in range(1, count + 1)]
    largest = limit if full else min(limit, max(-(-total // count), total * portions[0] // sum(portions)))
    least = 1 if total - largest >= count - 1 else 0
    counts, spare = [largest] + [least] * (count - 1), total - largest - least * (count - 1)
    while spare > 0:
        movable = [i for i in range(1, count) if counts[i] < largest] or [i for i in range(1, count) if counts[i] < limit]
        whole, budget = sum([portions[i] for i in movable]), spare
        for i in movable:
            more = min(limit - counts[i], max(1, budget * portions[i] // whole), spare)
            counts[i] = counts[i] + more
            spare = spare - more
    return np.array(counts)


def bell_draw(stream_key, shape, width, limit, cuts=(), kind=jnp.bfloat16):
    result = width * jax.random.normal(stream_key, shape, jnp.float32)
    if cuts:
        result = result * level_of(stream_key, shape, cuts, -0.22, 0.18)
    return jnp.clip(result, -limit, limit).astype(kind)


def setup_inputs(seed: int = 0) -> dict:
    key_of = jax.random.split(jax.random.key(seed), 7)
    tokens = bell_draw(key_of[0], (TOKENS, D), 1.0, 6.0, ((0, 32),))
    expert_ids_keys = jax.random.split(jax.random.fold_in(key_of[1], 1), TOKENS // TOK)
    expert_ids_turns = jax.random.permutation(jax.random.fold_in(key_of[1], 3), TOKENS // TOK)
    expert_ids = jax.vmap(lambda own, number: deal_out(jax.random.fold_in(key_of[1], 2), own, number, TOK, EXPERTS, TOP, CAP, 2))(expert_ids_keys, expert_ids_turns).reshape((TOKENS, TOP))
    route_weights = jnp.clip(0.05 + 0.39999999 * jax.random.uniform(key_of[2], (TOKENS, TOP), jnp.float32) ** level_of(key_of[2], (TOKENS, TOP), ((0, 32),), -0.2, 0.2), 0.05, 0.45)
    gate_up_panels = bell_draw(key_of[3], (EXPERTS, N_DP, D // 2, 2 * HID), D ** -0.5, 0.09375, ((0, 32), (1, 16)))
    down_panels = bell_draw(key_of[4], (EXPERTS, FF, D), FF ** -0.5, 0.1875, ((0, 32), (2, 16)))
    partner = draw_partner(jax.random.fold_in(key_of[6], 71), 0)
    return {"tokens": tokens, "expert_ids": expert_ids, "route_weights": route_weights, "gate_up_panels": gate_up_panels, "down_panels": down_panels, "partner": partner}


def unpack_panels(block):
    pair_count = N_DP // 2
    shaped = block.reshape(pair_count, 2, D // 2, 2, HID)
    shaped = jnp.transpose(shaped, (3, 1, 2, 0, 4))
    return shaped.reshape(2, D, FF)


def reference(tokens, expert_ids, route_weights, gate_up_panels, down_panels, partner):
    labels = jnp.arange(EXPERTS, dtype=jnp.int32)
    onehot = (expert_ids[:, :, None] == labels[None, None, :]).astype(jnp.int32)
    picked = jnp.sum(onehot, axis=1).astype(jnp.int32)
    grouped = picked.reshape(N_EXPERT, TOK, EXPERTS)
    slot_rank = (jnp.cumsum(grouped, axis=1).astype(jnp.int32) - grouped).reshape(TOKENS, EXPERTS)
    weight_table = jnp.sum(onehot.astype(jnp.float32) * route_weights[:, :, None], axis=1)
    group_of = (jnp.arange(TOKENS, dtype=jnp.int32) // TOK).astype(jnp.int32)
    padded = jnp.concatenate([tokens, jnp.zeros((1, D), tokens.dtype)], axis=0)
    dummy = N_EXPERT * CAP

    def per_expert(running, expert):
        panels = unpack_panels(lax.dynamic_index_in_dim(gate_up_panels, expert, 0, keepdims=False))
        down = lax.dynamic_index_in_dim(down_panels, expert, 0, keepdims=False)
        column = lax.dynamic_index_in_dim(picked, expert, 1, keepdims=False)
        rank_column = lax.dynamic_index_in_dim(slot_rank, expert, 1, keepdims=False)
        weight_column = lax.dynamic_index_in_dim(weight_table, expert, 1, keepdims=False)
        position = jnp.where(column > 0, group_of * CAP + rank_column, dummy).astype(jnp.int32)
        source = jnp.full((dummy + 1,), TOKENS, jnp.int32).at[position].set(jnp.arange(TOKENS, dtype=jnp.int32))
        buffer = padded[source[:dummy]]
        gate = jnp.dot(buffer, panels[0], preferred_element_type=jnp.float32)
        upward = jnp.dot(buffer, panels[1], preferred_element_type=jnp.float32)
        hidden = (jax.nn.silu(gate) * upward).astype(jnp.bfloat16)
        output = jnp.dot(hidden, down, preferred_element_type=jnp.float32).astype(jnp.bfloat16)
        output = jnp.concatenate([output, jnp.zeros((1, D), output.dtype)], axis=0)
        running = running + weight_column[:, None] * output[position].astype(jnp.float32)
        return running, None

    running, _ = lax.scan(per_expert, jnp.zeros((TOKENS, D), jnp.float32), labels)
    moe_out = running.astype(jnp.bfloat16)
    new_gate_up = jnp.take(gate_up_panels, partner, axis=0)
    new_down = jnp.take(down_panels, partner, axis=0)
    return (moe_out, new_gate_up, new_down)
```

```python
import jax
import jax.numpy as jnp
from jax import lax
from jax.sharding import PartitionSpec as P


def shift_route(axis, step):
    count = lax.axis_size(axis)
    return [(low, (low & ~3) | ((low + step) & 3)) for low in range(count)]


def swap_panels(gate_up, down, partner):
    here = lax.axis_index("expert")
    kind = jnp.bitwise_xor(partner[here], here)
    even = (here & 1) == 0
    gate_rows = gate_up.shape[2] // 2
    down_rows = down.shape[1] // 2
    first = (gate_up[:, :, :gate_rows], down[:, :down_rows])
    second = (gate_up[:, :, gate_rows:], down[:, down_rows:])
    ahead, behind = shift_route("expert", 1), shift_route("expert", 3)
    from_behind = lax.ppermute(first, "expert", ahead)
    from_ahead = lax.ppermute(second, "expert", behind)
    is_two = kind == 2

    def pick(flag, left, right):
        return tuple(jnp.where(flag, l, r) for l, r in zip(left, right))

    send_ahead = pick(is_two, from_behind, second)
    send_behind = pick(is_two, from_ahead, first)
    got_behind = lax.ppermute(send_ahead, "expert", ahead)
    got_ahead = lax.ppermute(send_behind, "expert", behind)
    one_even = (kind == 1) & even
    one_odd = (kind == 1) & ~even
    new_first = pick(is_two, got_behind, pick(one_even, got_ahead, pick(one_odd, from_behind, first)))
    new_second = pick(is_two, got_ahead, pick(one_even, from_ahead, pick(one_odd, got_behind, second)))
    new_gate_up = jnp.concatenate([new_first[0], new_second[0]], axis=2)
    new_down = jnp.concatenate([new_first[1], new_second[1]], axis=1)
    return (new_gate_up, new_down)


def run_layer(tokens, expert_ids, route_weights, gate_up, down):
    devices = lax.axis_size("expert")
    token_rows, model_width = tokens.shape
    top_count = expert_ids.shape[1]
    expert_count = devices
    capacity = min(token_rows, 3 * token_rows * top_count // (2 * expert_count))
    half_width = model_width // 2
    side = lax.rem(lax.axis_index("dp"), 2)
    own_half = lax.dynamic_slice_in_dim(tokens, side * half_width, half_width, 1)
    labels = jnp.arange(expert_count, dtype=jnp.int32)
    onehot = (expert_ids[:, :, None] == labels[None, None, :]).astype(jnp.int32)
    picked = jnp.sum(onehot, axis=1)
    slot_rank = jnp.cumsum(picked, axis=0) - picked
    slots = jnp.sum(onehot * slot_rank[:, None, :], axis=2)
    place = (expert_ids * capacity + slots).reshape(-1)
    row_ids = jnp.repeat(jnp.arange(token_rows, dtype=jnp.int32), top_count)
    source = jnp.full((devices * capacity,), token_rows, jnp.int32).at[place].set(row_ids)
    padded = jnp.concatenate([own_half, jnp.zeros((1, half_width), own_half.dtype)], axis=0)
    outgoing = padded[source].reshape(devices, capacity, half_width)
    arrived = lax.all_to_all(outgoing, "expert", split_axis=0, concat_axis=0, tiled=True)
    flat = arrived.reshape(devices * capacity, half_width)
    partial_value = jnp.dot(flat, gate_up, preferred_element_type=jnp.float32)
    half_rows = flat.shape[0] // 2
    mine = lax.dynamic_slice_in_dim(partial_value, side * half_rows, half_rows, 0)
    other = lax.dynamic_slice_in_dim(partial_value, (1 - side) * half_rows, half_rows, 0)
    route = [(low, low ^ 1) for low in range(lax.axis_size("dp"))]
    summed = mine + lax.ppermute(other, "dp", route)
    block_units = gate_up.shape[1] // 2
    hidden = (jax.nn.silu(summed[:, :block_units]) * summed[:, block_units:]).astype(jnp.bfloat16)
    gathered = lax.all_gather(hidden, "dp", axis=0, tiled=False)
    pair_count = lax.axis_size("dp") // 2
    out_columns = down.shape[1]
    outputs = jnp.einsum(
        "qhrk,qkc->hrc",
        gathered.reshape(pair_count, 2, half_rows, block_units),
        down.reshape(pair_count, block_units, out_columns),
        preferred_element_type=jnp.float32,
    )
    expert_out = outputs.reshape(devices, capacity, out_columns).astype(jnp.bfloat16)
    returned = lax.all_to_all(expert_out, "expert", split_axis=0, concat_axis=0, tiled=True)
    chosen = returned.reshape(devices * capacity, out_columns)[place].reshape(
        token_rows, top_count, out_columns
    )
    mixed = jnp.sum(chosen.astype(jnp.float32) * route_weights[:, :, None], axis=1)
    return mixed.astype(jnp.bfloat16)


def per_device(tokens, expert_ids, route_weights, gate_up_panels, down_panels, partner):
    moe_out = run_layer(tokens, expert_ids, route_weights, gate_up_panels[0, 0], down_panels[0])
    new_gate_up, new_down = swap_panels(gate_up_panels, down_panels, partner)
    return (moe_out, new_gate_up, new_down)


def solution(mesh):
    return jax.shard_map(
        per_device,
        mesh=mesh,
        in_specs=(
            P("expert", None),
            P("expert", None),
            P("expert", None),
            P("expert", "dp", None, None),
            P("expert", None, "dp"),
            P(),
        ),
        out_specs=(P("expert", "dp"), P("expert", "dp", None, None), P("expert", None, "dp")),
        check_vma=False,
    )
```

```python
import jax
import jax.numpy as jnp
from jax import lax
from jax.sharding import Mesh
from jax.sharding import PartitionSpec as P

EXPERT = ("y", "zhi", "x")
DP = ("zlo", "core")
FLIP = [(0, 1), (1, 0)]


def swap_panels(gate_up, down, partner):
    here = lax.axis_index(EXPERT)
    kind = jnp.bitwise_xor(partner[here], here)
    even = (lax.axis_index("x") & 1) == 0
    gate_rows = gate_up.shape[2] // 2
    down_rows = down.shape[1] // 2
    first = (gate_up[:, :, :gate_rows], down[:, :down_rows])
    second = (gate_up[:, :, gate_rows:], down[:, down_rows:])
    ring = lax.axis_size("x")
    ahead = [(i, (i + 1) % ring) for i in range(ring)]
    behind = [(i, (i + ring - 1) % ring) for i in range(ring)]
    from_behind = lax.ppermute(first, "x", ahead)
    from_ahead = lax.ppermute(second, "x", behind)
    is_two = kind == 2

    def pick(flag, left, right):
        return tuple(jnp.where(flag, l, r) for l, r in zip(left, right))

    send_ahead = pick(is_two, from_behind, second)
    send_behind = pick(is_two, from_ahead, first)
    got_behind = lax.ppermute(send_ahead, "x", ahead)
    got_ahead = lax.ppermute(send_behind, "x", behind)
    one_even = (kind == 1) & even
    one_odd = (kind == 1) & ~even
    new_first = pick(is_two, got_behind, pick(one_even, got_ahead, pick(one_odd, from_behind, first)))
    new_second = pick(is_two, got_ahead, pick(one_even, from_ahead, pick(one_odd, got_behind, second)))
    new_gate_up = jnp.concatenate([new_first[0], new_second[0]], axis=2)
    new_down = jnp.concatenate([new_first[1], new_second[1]], axis=1)
    return (new_gate_up, new_down)


def run_layer(tokens, expert_ids, route_weights, gate_up, down):
    rows_y, rows_x = lax.axis_size("y"), lax.axis_size("x")
    lines = rows_y * rows_x
    expert_count = 2 * lines
    chunks = lax.axis_size("zlo")
    token_rows, model_width = tokens.shape
    top_count = expert_ids.shape[1]
    capacity = min(token_rows, 3 * token_rows * top_count // (2 * expert_count))
    half_width = model_width // 2
    chunk_width = half_width // chunks
    side = lax.axis_index("core")
    zhi = lax.axis_index("zhi")
    own_half = lax.dynamic_slice_in_dim(tokens, side * half_width, half_width, 1)
    own_chunk = lax.dynamic_slice_in_dim(
        tokens, side * half_width + lax.axis_index("zlo") * chunk_width, chunk_width, 1
    )
    labels = jnp.arange(expert_count, dtype=jnp.int32)
    onehot = (expert_ids[:, :, None] == labels[None, None, :]).astype(jnp.int32)
    picked = jnp.sum(onehot, axis=1)
    slot_rank = jnp.cumsum(picked, axis=0) - picked
    slots = jnp.sum(onehot * slot_rank[:, None, :], axis=2)
    place = (expert_ids * capacity + slots).reshape(-1)
    row_ids = jnp.repeat(jnp.arange(token_rows, dtype=jnp.int32), top_count)
    source = jnp.full((expert_count * capacity,), token_rows, jnp.int32).at[place].set(row_ids)
    source = source.reshape(rows_y, 2, rows_x, capacity)
    near_source = lax.dynamic_index_in_dim(source, zhi, 1, keepdims=False).reshape(-1)
    far_source = lax.dynamic_index_in_dim(source, 1 - zhi, 1, keepdims=False).reshape(-1)
    padded_half = jnp.concatenate([own_half, jnp.zeros((1, half_width), tokens.dtype)], axis=0)
    padded_chunk = jnp.concatenate([own_chunk, jnp.zeros((1, chunk_width), tokens.dtype)], axis=0)
    near_out = padded_half[near_source].reshape(lines, capacity, half_width)
    far_out = padded_chunk[far_source].reshape(lines, capacity, chunk_width)
    near_in = lax.all_to_all(near_out, ("y", "x"), 0, 0, tiled=True)
    far_mid = lax.ppermute(far_out, "zhi", FLIP)
    far_in = lax.all_to_all(far_mid, ("y", "x"), 0, 0, tiled=True)
    far_full = lax.all_gather(far_in, "zlo", axis=0, tiled=False)
    part_rows = lines * capacity
    near_value = jnp.dot(near_in.reshape(part_rows, half_width), gate_up, preferred_element_type=jnp.float32)
    far_value = jnp.einsum(
        "cnf,cfu->nu",
        far_full.reshape(chunks, part_rows, chunk_width),
        gate_up.reshape(chunks, chunk_width, gate_up.shape[1]),
        preferred_element_type=jnp.float32,
    )
    keep_near = side == 0
    mine = jnp.where(keep_near, near_value, far_value)
    other = jnp.where(keep_near, far_value, near_value)
    summed = mine + lax.ppermute(other, "core", FLIP)
    block_units = gate_up.shape[1] // 2
    hidden = (jax.nn.silu(summed[:, :block_units]) * summed[:, block_units:]).astype(jnp.bfloat16)
    gathered = lax.all_gather(hidden, "zlo", axis=0, tiled=False)
    partner_part = lax.ppermute(gathered, "core", FLIP)
    near_hidden = jnp.where(keep_near, gathered, partner_part)
    far_hidden = jnp.where(keep_near, partner_part, gathered)
    out_columns = down.shape[1]
    down_blocks = down.reshape(chunks, block_units, out_columns)

    def project(hidden_part):
        value = jnp.einsum("qrk,qkc->rc", hidden_part, down_blocks, preferred_element_type=jnp.float32)
        return value.astype(jnp.bfloat16).reshape(lines, capacity, out_columns)

    near_back = lax.all_to_all(project(near_hidden), ("y", "x"), 0, 0, tiled=True)
    far_back = lax.ppermute(lax.all_to_all(project(far_hidden), ("y", "x"), 0, 0, tiled=True), "zhi", FLIP)
    near_back = near_back.reshape(rows_y, rows_x, capacity, out_columns)
    far_back = far_back.reshape(rows_y, rows_x, capacity, out_columns)
    low_first = zhi == 0
    returned = jnp.stack(
        [jnp.where(low_first, near_back, far_back), jnp.where(low_first, far_back, near_back)], axis=1
    )
    chosen = returned.reshape(expert_count * capacity, out_columns)[place].reshape(
        token_rows, top_count, out_columns
    )
    mixed = jnp.sum(chosen.astype(jnp.float32) * route_weights[:, :, None], axis=1)
    return mixed.astype(jnp.bfloat16)


def per_device(tokens, expert_ids, route_weights, gate_up_panels, down_panels, partner):
    moe_out = run_layer(tokens, expert_ids, route_weights, gate_up_panels[0, 0], down_panels[0])
    new_gate_up, new_down = swap_panels(gate_up_panels, down_panels, partner)
    return (moe_out, new_gate_up, new_down)


def solution(mesh):
    experts, dps = mesh.devices.shape
    layout = mesh.devices.reshape(experts // 8, 2, 4, dps // 2, 2)
    split = Mesh(layout, EXPERT + DP)
    return jax.shard_map(
        per_device,
        mesh=split,
        in_specs=(
            P(EXPERT, None),
            P(EXPERT, None),
            P(EXPERT, None),
            P(EXPERT, DP, None, None),
            P(EXPERT, None, DP),
            P(),
        ),
        out_specs=(P(EXPERT, DP), P(EXPERT, DP, None, None), P(EXPERT, None, DP)),
        check_vma=False,
    )
```

```python
import jax
import jax.numpy as jnp
from jax import lax
from jax.sharding import Mesh
from jax.sharding import PartitionSpec as P

EXPERT = ("y", "zhi", "x")
DP = ("zlo", "core")
FLIP = [(0, 1), (1, 0)]


def swap_panels(gate_up, down, partner):
    here = lax.axis_index(EXPERT)
    kind = jnp.bitwise_xor(partner[here], here)
    even = (lax.axis_index("x") & 1) == 0
    gate_rows = gate_up.shape[2] // 2
    down_rows = down.shape[1] // 2
    first = (gate_up[:, :, :gate_rows], down[:, :down_rows])
    second = (gate_up[:, :, gate_rows:], down[:, down_rows:])
    ring = lax.axis_size("x")
    ahead = [(i, (i + 1) % ring) for i in range(ring)]
    behind = [(i, (i + ring - 1) % ring) for i in range(ring)]
    from_behind = lax.ppermute(first, "x", ahead)
    from_ahead = lax.ppermute(second, "x", behind)
    is_two = kind == 2

    def pick(flag, left, right):
        return tuple(jnp.where(flag, l, r) for l, r in zip(left, right))

    send_ahead = pick(is_two, from_behind, second)
    send_behind = pick(is_two, from_ahead, first)
    got_behind = lax.ppermute(send_ahead, "x", ahead)
    got_ahead = lax.ppermute(send_behind, "x", behind)
    one_even = (kind == 1) & even
    one_odd = (kind == 1) & ~even
    new_first = pick(is_two, got_behind, pick(one_even, got_ahead, pick(one_odd, from_behind, first)))
    new_second = pick(is_two, got_ahead, pick(one_even, from_ahead, pick(one_odd, got_behind, second)))
    new_gate_up = jnp.concatenate([new_first[0], new_second[0]], axis=2)
    new_down = jnp.concatenate([new_first[1], new_second[1]], axis=1)
    return (new_gate_up, new_down)


def routing(expert_ids, expert_count, capacity):
    token_rows, top_count = expert_ids.shape
    labels = jnp.arange(expert_count, dtype=jnp.int32)
    onehot = (expert_ids[:, :, None] == labels[None, None, :]).astype(jnp.int32)
    picked = jnp.sum(onehot, axis=1)
    slot_rank = jnp.cumsum(picked, axis=0) - picked
    slots = jnp.sum(onehot * slot_rank[:, None, :], axis=2)
    place = (expert_ids * capacity + slots).reshape(-1)
    row_ids = jnp.repeat(jnp.arange(token_rows, dtype=jnp.int32), top_count)
    source = jnp.full((expert_count * capacity,), token_rows, jnp.int32).at[place].set(row_ids)
    return slots, source


def combine(table, expert_ids, slots, weights, zhi, rows_x, capacity):
    in_half = (expert_ids // rows_x) % 2 == zhi
    line = (expert_ids // (2 * rows_x)) * rows_x + expert_ids % rows_x
    blank = table.shape[0]
    index = jnp.where(in_half, line * capacity + slots, blank)
    padded = jnp.concatenate([table, jnp.zeros((1, table.shape[1]), table.dtype)], axis=0)
    chosen = padded[index.reshape(-1)].reshape(index.shape + (table.shape[1],))
    return jnp.sum(chosen.astype(jnp.float32) * weights[:, :, None], axis=1)


def run_layer(tokens, expert_ids, route_weights, gate_up, down):
    rows_y, rows_x = lax.axis_size("y"), lax.axis_size("x")
    lines = rows_y * rows_x
    expert_count = 2 * lines
    chunks = lax.axis_size("zlo")
    token_rows, model_width = tokens.shape
    top_count = expert_ids.shape[1]
    capacity = min(token_rows, 3 * token_rows * top_count // (2 * expert_count))
    half_width = model_width // 2
    side = lax.axis_index("core")
    zhi = lax.axis_index("zhi")
    own_half = lax.dynamic_slice_in_dim(tokens, side * half_width, half_width, 1)
    far_half, far_ids, far_weights = lax.ppermute((own_half, expert_ids, route_weights), "zhi", FLIP)
    own_slots, own_source = routing(expert_ids, expert_count, capacity)
    far_slots, far_source = routing(far_ids, expert_count, capacity)

    def outgoing(rows, source):
        near = lax.dynamic_index_in_dim(source.reshape(rows_y, 2, rows_x, capacity), zhi, 1, keepdims=False)
        padded = jnp.concatenate([rows, jnp.zeros((1, half_width), rows.dtype)], axis=0)
        return padded[near.reshape(-1)].reshape(lines, 1, capacity, half_width)

    sent = jnp.concatenate([outgoing(own_half, own_source), outgoing(far_half, far_source)], axis=1)
    arrived = lax.all_to_all(sent, ("y", "x"), 0, 0, tiled=True)
    total_rows = lines * 2 * capacity
    half_rows = total_rows // 2
    partial_value = jnp.dot(arrived.reshape(total_rows, half_width), gate_up, preferred_element_type=jnp.float32)
    mine = lax.dynamic_slice_in_dim(partial_value, side * half_rows, half_rows, 0)
    other = lax.dynamic_slice_in_dim(partial_value, (1 - side) * half_rows, half_rows, 0)
    summed = mine + lax.ppermute(other, "core", FLIP)
    block_units = gate_up.shape[1] // 2
    hidden = (jax.nn.silu(summed[:, :block_units]) * summed[:, block_units:]).astype(jnp.bfloat16)
    gathered = lax.all_gather(hidden, "zlo", axis=0, tiled=False)
    partner_part = lax.ppermute(gathered, "core", FLIP)
    keep_first = side == 0
    first_hidden = jnp.where(keep_first, gathered, partner_part)
    second_hidden = jnp.where(keep_first, partner_part, gathered)
    out_columns = down.shape[1]
    down_blocks = down.reshape(chunks, block_units, out_columns)

    def project(hidden_part):
        value = jnp.einsum("qrk,qkc->rc", hidden_part, down_blocks, preferred_element_type=jnp.float32)
        return value.astype(jnp.bfloat16)

    expert_out = jnp.concatenate([project(first_hidden), project(second_hidden)], axis=0)
    returned = lax.all_to_all(expert_out.reshape(lines, 2, capacity, out_columns), ("y", "x"), 0, 0, tiled=True)
    own_table = returned[:, 0].reshape(lines * capacity, out_columns)
    far_table = returned[:, 1].reshape(lines * capacity, out_columns)
    far_sum = combine(far_table, far_ids, far_slots, far_weights, zhi, rows_x, capacity)
    own_sum = combine(own_table, expert_ids, own_slots, route_weights, zhi, rows_x, capacity)
    mixed = own_sum + lax.ppermute(far_sum, "zhi", FLIP)
    return mixed.astype(jnp.bfloat16)


def per_device(tokens, expert_ids, route_weights, gate_up_panels, down_panels, partner):
    moe_out = run_layer(tokens, expert_ids, route_weights, gate_up_panels[0, 0], down_panels[0])
    new_gate_up, new_down = swap_panels(gate_up_panels, down_panels, partner)
    return (moe_out, new_gate_up, new_down)


def solution(mesh):
    experts, dps = mesh.devices.shape
    layout = mesh.devices.reshape(experts // 8, 2, 4, dps // 2, 2)
    split = Mesh(layout, EXPERT + DP)
    return jax.shard_map(
        per_device,
        mesh=split,
        in_specs=(
            P(EXPERT, None),
            P(EXPERT, None),
            P(EXPERT, None),
            P(EXPERT, DP, None, None),
            P(EXPERT, None, DP),
            P(),
        ),
        out_specs=(P(EXPERT, DP), P(EXPERT, DP, None, None), P(EXPERT, None, DP)),
        check_vma=False,
    )
```

```python
import jax
import jax.numpy as jnp
from jax import lax
from jax.sharding import Mesh
from jax.sharding import PartitionSpec as P

EXPERT = ("y", "zhi", "x")
DP = ("zlo", "core")
FLIP = [(0, 1), (1, 0)]


def swap_panels(gate_up, down, partner):
    here = lax.axis_index(EXPERT)
    kind = jnp.bitwise_xor(partner[here], here)
    even = (lax.axis_index("x") & 1) == 0
    gate_rows = gate_up.shape[2] // 2
    down_rows = down.shape[1] // 2
    first = (gate_up[:, :, :gate_rows], down[:, :down_rows])
    second = (gate_up[:, :, gate_rows:], down[:, down_rows:])
    ring = lax.axis_size("x")
    ahead = [(i, (i + 1) % ring) for i in range(ring)]
    behind = [(i, (i + ring - 1) % ring) for i in range(ring)]
    from_behind = lax.ppermute(first, "x", ahead)
    from_ahead = lax.ppermute(second, "x", behind)
    is_two = kind == 2

    def pick(flag, left, right):
        return tuple(jnp.where(flag, l, r) for l, r in zip(left, right))

    send_ahead = pick(is_two, from_behind, second)
    send_behind = pick(is_two, from_ahead, first)
    got_behind = lax.ppermute(send_ahead, "x", ahead)
    got_ahead = lax.ppermute(send_behind, "x", behind)
    one_even = (kind == 1) & even
    one_odd = (kind == 1) & ~even
    new_first = pick(is_two, got_behind, pick(one_even, got_ahead, pick(one_odd, from_behind, first)))
    new_second = pick(is_two, got_ahead, pick(one_even, from_ahead, pick(one_odd, got_behind, second)))
    new_gate_up = jnp.concatenate([new_first[0], new_second[0]], axis=2)
    new_down = jnp.concatenate([new_first[1], new_second[1]], axis=1)
    return (new_gate_up, new_down)


def routing(expert_ids, expert_count, capacity):
    token_rows, top_count = expert_ids.shape
    labels = jnp.arange(expert_count, dtype=jnp.int32)
    onehot = (expert_ids[:, :, None] == labels[None, None, :]).astype(jnp.int32)
    picked = jnp.sum(onehot, axis=1)
    slot_rank = jnp.cumsum(picked, axis=0) - picked
    slots = jnp.sum(onehot * slot_rank[:, None, :], axis=2)
    place = (expert_ids * capacity + slots).reshape(-1)
    row_ids = jnp.repeat(jnp.arange(token_rows, dtype=jnp.int32), top_count)
    source = jnp.full((expert_count * capacity,), token_rows, jnp.int32).at[place].set(row_ids)
    return slots, source


def combine(table, expert_ids, slots, weights, zhi, rows_x, capacity):
    in_half = (expert_ids // rows_x) % 2 == zhi
    line = (expert_ids // (2 * rows_x)) * rows_x + expert_ids % rows_x
    blank = table.shape[0]
    index = jnp.where(in_half, line * capacity + slots, blank)
    padded = jnp.concatenate([table, jnp.zeros((1, table.shape[1]), table.dtype)], axis=0)
    chosen = padded[index.reshape(-1)].reshape(index.shape + (table.shape[1],))
    return jnp.sum(chosen.astype(jnp.float32) * weights[:, :, None], axis=1)


def run_layer(tokens, expert_ids, route_weights, gate_up, down):
    rows_y, rows_x = lax.axis_size("y"), lax.axis_size("x")
    lines = rows_y * rows_x
    expert_count = 2 * lines
    chunks = lax.axis_size("zlo")
    token_rows, model_width = tokens.shape
    top_count = expert_ids.shape[1]
    capacity = min(token_rows, 3 * token_rows * top_count // (2 * expert_count))
    half_width = model_width // 2
    side = lax.axis_index("core")
    zhi = lax.axis_index("zhi")
    own_half = lax.dynamic_slice_in_dim(tokens, side * half_width, half_width, 1)
    mirror = [(high * chunks + low, (1 - high) * chunks + chunks - 1 - low) for high in range(2) for low in range(chunks)]
    far_half, far_ids, far_weights = lax.ppermute((own_half, expert_ids, route_weights), ("zhi", "zlo"), mirror)
    own_slots, own_source = routing(expert_ids, expert_count, capacity)
    far_slots, far_source = routing(far_ids, expert_count, capacity)
    out_columns = down.shape[1]
    block_units = gate_up.shape[1] // 2
    down_blocks = down.reshape(chunks, block_units, out_columns)
    keep_first = side == 0

    def project(hidden_part):
        value = jnp.einsum("qrk,qkc->rc", hidden_part, down_blocks, preferred_element_type=jnp.float32)
        return value.astype(jnp.bfloat16)

    def dispatch(rows, source):
        near = lax.dynamic_index_in_dim(source.reshape(rows_y, 2, rows_x, capacity), zhi, 1, keepdims=False)
        padded = jnp.concatenate([rows, jnp.zeros((1, half_width), rows.dtype)], axis=0)
        sent = padded[near.reshape(-1)].reshape(lines, capacity, half_width)
        return lax.all_to_all(sent, ("y", "x"), 0, 0, tiled=True)

    def experts(arrived):
        part_rows = lines * capacity
        half_rows = part_rows // 2
        partial_value = jnp.dot(arrived.reshape(part_rows, half_width), gate_up, preferred_element_type=jnp.float32)
        mine = lax.dynamic_slice_in_dim(partial_value, side * half_rows, half_rows, 0)
        other = lax.dynamic_slice_in_dim(partial_value, (1 - side) * half_rows, half_rows, 0)
        summed = mine + lax.ppermute(other, "core", FLIP)
        hidden = (jax.nn.silu(summed[:, :block_units]) * summed[:, block_units:]).astype(jnp.bfloat16)
        gathered = lax.all_gather(hidden, "zlo", axis=0, tiled=False)
        partner_part = lax.ppermute(gathered, "core", FLIP)
        first_hidden = jnp.where(keep_first, gathered, partner_part)
        second_hidden = jnp.where(keep_first, partner_part, gathered)
        expert_out = jnp.concatenate([project(first_hidden), project(second_hidden)], axis=0)
        back = lax.all_to_all(expert_out.reshape(lines, capacity, out_columns), ("y", "x"), 0, 0, tiled=True)
        return back.reshape(lines * capacity, out_columns)

    own_arrived = dispatch(own_half, own_source)
    far_arrived = dispatch(far_half, far_source)
    own_table = experts(own_arrived)
    far_table = experts(far_arrived)
    far_sum = combine(far_table, far_ids, far_slots, far_weights, zhi, rows_x, capacity)
    own_sum = combine(own_table, expert_ids, own_slots, route_weights, zhi, rows_x, capacity)
    mixed = own_sum + lax.ppermute(far_sum, "zhi", FLIP)
    return mixed.astype(jnp.bfloat16), far_arrived


def per_device(tokens, expert_ids, route_weights, gate_up_panels, down_panels, partner):
    moe_out, anchor = run_layer(tokens, expert_ids, route_weights, gate_up_panels[0, 0], down_panels[0])
    gate_up_late, down_late, _ = lax.optimization_barrier((gate_up_panels, down_panels, anchor))
    new_gate_up, new_down = swap_panels(gate_up_late, down_late, partner)
    return (moe_out, new_gate_up, new_down)


def solution(mesh):
    experts, dps = mesh.devices.shape
    layout = mesh.devices.reshape(experts // 8, 2, 4, dps // 2, 2)
    split = Mesh(layout, EXPERT + DP)
    return jax.shard_map(
        per_device,
        mesh=split,
        in_specs=(
            P(EXPERT, None),
            P(EXPERT, None),
            P(EXPERT, None),
            P(EXPERT, DP, None, None),
            P(EXPERT, None, DP),
            P(),
        ),
        out_specs=(P(EXPERT, DP), P(EXPERT, DP, None, None), P(EXPERT, None, DP)),
        check_vma=False,
    )
```

```python
import jax
import jax.numpy as jnp
from jax import lax
from jax.sharding import Mesh
from jax.sharding import PartitionSpec as P

EXPERT = ("y", "zhi", "x")
DP = ("zlo", "core")
FLIP = [(0, 1), (1, 0)]


def swap_panels(gate_up, down, partner):
    here = lax.axis_index(EXPERT)
    kind = jnp.bitwise_xor(partner[here], here)
    even = (lax.axis_index("x") & 1) == 0
    gate_rows = gate_up.shape[2] // 2
    down_rows = down.shape[1] // 2
    first = (gate_up[:, :, :gate_rows], down[:, :down_rows])
    second = (gate_up[:, :, gate_rows:], down[:, down_rows:])
    ring = lax.axis_size("x")
    ahead = [(i, (i + 1) % ring) for i in range(ring)]
    behind = [(i, (i + ring - 1) % ring) for i in range(ring)]
    from_behind = lax.ppermute(first, "x", ahead)
    from_ahead = lax.ppermute(second, "x", behind)
    is_two = kind == 2

    def pick(flag, left, right):
        return tuple(jnp.where(flag, l, r) for l, r in zip(left, right))

    send_ahead = pick(is_two, from_behind, second)
    send_behind = pick(is_two, from_ahead, first)
    got_behind = lax.ppermute(send_ahead, "x", ahead)
    got_ahead = lax.ppermute(send_behind, "x", behind)
    one_even = (kind == 1) & even
    one_odd = (kind == 1) & ~even
    new_first = pick(is_two, got_behind, pick(one_even, got_ahead, pick(one_odd, from_behind, first)))
    new_second = pick(is_two, got_ahead, pick(one_even, from_ahead, pick(one_odd, got_behind, second)))
    new_gate_up = jnp.concatenate([new_first[0], new_second[0]], axis=2)
    new_down = jnp.concatenate([new_first[1], new_second[1]], axis=1)
    return (new_gate_up, new_down)


def gather_line(block):
    count = lax.axis_size("zlo")
    spread = jnp.broadcast_to(block[None], (count,) + block.shape)
    return lax.all_to_all(spread, "zlo", 0, 0, tiled=True)


def routing(expert_ids, expert_count, capacity):
    token_rows, top_count = expert_ids.shape
    labels = jnp.arange(expert_count, dtype=jnp.int32)
    onehot = (expert_ids[:, :, None] == labels[None, None, :]).astype(jnp.int32)
    picked = jnp.sum(onehot, axis=1)
    slot_rank = jnp.cumsum(picked, axis=0) - picked
    slots = jnp.sum(onehot * slot_rank[:, None, :], axis=2)
    place = (expert_ids * capacity + slots).reshape(-1)
    row_ids = jnp.repeat(jnp.arange(token_rows, dtype=jnp.int32), top_count)
    source = jnp.full((expert_count * capacity,), token_rows, jnp.int32).at[place].set(row_ids)
    return slots, source


def combine(table, expert_ids, slots, weights, zhi, rows_x, capacity):
    in_half = (expert_ids // rows_x) % 2 == zhi
    line = (expert_ids // (2 * rows_x)) * rows_x + expert_ids % rows_x
    blank = table.shape[0]
    index = jnp.where(in_half, line * capacity + slots, blank)
    padded = jnp.concatenate([table, jnp.zeros((1, table.shape[1]), table.dtype)], axis=0)
    chosen = padded[index.reshape(-1)].reshape(index.shape + (table.shape[1],))
    return jnp.sum(chosen.astype(jnp.float32) * weights[:, :, None], axis=1)


def run_layer(tokens, expert_ids, route_weights, gate_up, down, swapped):
    rows_y, rows_x = lax.axis_size("y"), lax.axis_size("x")
    lines = rows_y * rows_x
    expert_count = 2 * lines
    chunks = lax.axis_size("zlo")
    token_rows, model_width = tokens.shape
    top_count = expert_ids.shape[1]
    capacity = min(token_rows, 3 * token_rows * top_count // (2 * expert_count))
    half_width = model_width // 2
    side = lax.axis_index("core")
    zhi = lax.axis_index("zhi")
    chunk_width = half_width // chunks
    own_half = lax.dynamic_slice_in_dim(tokens, side * half_width, half_width, 1)
    own_chunk = lax.dynamic_slice_in_dim(
        tokens, side * half_width + lax.axis_index("zlo") * chunk_width, chunk_width, 1
    )
    mirror = [(high * chunks + low, (1 - high) * chunks + chunks - 1 - low) for high in range(2) for low in range(chunks)]
    far_chunk, far_ids, far_weights = lax.ppermute((own_chunk, expert_ids, route_weights), ("zhi", "zlo"), mirror)
    far_chunks = gather_line(far_chunk)[::-1]
    far_half = jnp.transpose(far_chunks, (1, 0, 2)).reshape(token_rows, half_width)
    own_slots, own_source = routing(expert_ids, expert_count, capacity)
    far_slots, far_source = routing(far_ids, expert_count, capacity)
    out_columns = down.shape[1]
    block_units = gate_up.shape[1] // 2
    down_blocks = down.reshape(chunks, block_units, out_columns)
    keep_first = side == 0

    def project(hidden_part):
        value = jnp.einsum("qrk,qkc->rc", hidden_part, down_blocks, preferred_element_type=jnp.float32)
        return value.astype(jnp.bfloat16)

    def dispatch(rows, source):
        near = lax.dynamic_index_in_dim(source.reshape(rows_y, 2, rows_x, capacity), zhi, 1, keepdims=False)
        padded = jnp.concatenate([rows, jnp.zeros((1, half_width), rows.dtype)], axis=0)
        sent = padded[near.reshape(-1)].reshape(lines, capacity, half_width)
        return lax.all_to_all(sent, ("y", "x"), 0, 0, tiled=True)

    def experts(arrived):
        part_rows = lines * capacity
        half_rows = part_rows // 2
        partial_value = jnp.dot(arrived.reshape(part_rows, half_width), gate_up, preferred_element_type=jnp.float32)
        mine = lax.dynamic_slice_in_dim(partial_value, side * half_rows, half_rows, 0)
        other = lax.dynamic_slice_in_dim(partial_value, (1 - side) * half_rows, half_rows, 0)
        summed = mine + lax.ppermute(other, "core", FLIP)
        hidden = (jax.nn.silu(summed[:, :block_units]) * summed[:, block_units:]).astype(jnp.bfloat16)
        gathered = gather_line(hidden)
        partner_part = lax.ppermute(gathered, "core", FLIP)
        first_hidden = jnp.where(keep_first, gathered, partner_part)
        second_hidden = jnp.where(keep_first, partner_part, gathered)
        expert_out = jnp.concatenate([project(first_hidden), project(second_hidden)], axis=0)
        back = lax.all_to_all(expert_out.reshape(lines, capacity, out_columns), ("y", "x"), 0, 0, tiled=True)
        return back.reshape(lines * capacity, out_columns)

    own_arrived = dispatch(own_half, own_source)
    far_arrived = dispatch(far_half, far_source)
    own_arrived, swapped = lax.optimization_barrier((own_arrived, swapped))
    own_table = experts(own_arrived)
    far_table = experts(far_arrived)
    far_sum = combine(far_table, far_ids, far_slots, far_weights, zhi, rows_x, capacity)
    own_sum = combine(own_table, expert_ids, own_slots, route_weights, zhi, rows_x, capacity)
    mixed = own_sum + lax.ppermute(far_sum, "zhi", FLIP)
    return mixed.astype(jnp.bfloat16), swapped


def per_device(tokens, expert_ids, route_weights, gate_up_panels, down_panels, partner):
    swapped = swap_panels(gate_up_panels, down_panels, partner)
    moe_out, (new_gate_up, new_down) = run_layer(
        tokens, expert_ids, route_weights, gate_up_panels[0, 0], down_panels[0], swapped
    )
    return (moe_out, new_gate_up, new_down)


def solution(mesh):
    experts, dps = mesh.devices.shape
    layout = mesh.devices.reshape(experts // 8, 2, 4, dps // 2, 2)
    split = Mesh(layout, EXPERT + DP)
    return jax.shard_map(
        per_device,
        mesh=split,
        in_specs=(
            P(EXPERT, None),
            P(EXPERT, None),
            P(EXPERT, None),
            P(EXPERT, DP, None, None),
            P(EXPERT, None, DP),
            P(),
        ),
        out_specs=(P(EXPERT, DP), P(EXPERT, DP, None, None), P(EXPERT, None, DP)),
        check_vma=False,
    )
```

```python
import jax
import jax.numpy as jnp
from jax import lax
from jax.sharding import Mesh
from jax.sharding import PartitionSpec as P

EXPERT = ("y", "zhi", "x")
DP = ("zlo", "core")
FLIP = [(0, 1), (1, 0)]


def swap_panels(gate_up, down, partner):
    here = lax.axis_index(EXPERT)
    kind = jnp.bitwise_xor(partner[here], here)
    even = (lax.axis_index("x") & 1) == 0
    gate_rows = gate_up.shape[2] // 2
    down_rows = down.shape[1] // 2
    first = (gate_up[:, :, :gate_rows], down[:, :down_rows])
    second = (gate_up[:, :, gate_rows:], down[:, down_rows:])
    ring = lax.axis_size("x")
    ahead = [(i, (i + 1) % ring) for i in range(ring)]
    behind = [(i, (i + ring - 1) % ring) for i in range(ring)]
    from_behind = lax.ppermute(first, "x", ahead)
    from_ahead = lax.ppermute(second, "x", behind)
    is_two = kind == 2

    def pick(flag, left, right):
        return tuple(jnp.where(flag, l, r) for l, r in zip(left, right))

    send_ahead = pick(is_two, from_behind, second)
    send_behind = pick(is_two, from_ahead, first)
    got_behind = lax.ppermute(send_ahead, "x", ahead)
    got_ahead = lax.ppermute(send_behind, "x", behind)
    one_even = (kind == 1) & even
    one_odd = (kind == 1) & ~even
    new_first = pick(is_two, got_behind, pick(one_even, got_ahead, pick(one_odd, from_behind, first)))
    new_second = pick(is_two, got_ahead, pick(one_even, from_ahead, pick(one_odd, got_behind, second)))
    new_gate_up = jnp.concatenate([new_first[0], new_second[0]], axis=2)
    new_down = jnp.concatenate([new_first[1], new_second[1]], axis=1)
    return (new_gate_up, new_down)


def routing(expert_ids, expert_count, capacity):
    token_rows, top_count = expert_ids.shape
    labels = jnp.arange(expert_count, dtype=jnp.int32)
    onehot = (expert_ids[:, :, None] == labels[None, None, :]).astype(jnp.int32)
    picked = jnp.sum(onehot, axis=1)
    slot_rank = jnp.cumsum(picked, axis=0) - picked
    slots = jnp.sum(onehot * slot_rank[:, None, :], axis=2)
    place = (expert_ids * capacity + slots).reshape(-1)
    row_ids = jnp.repeat(jnp.arange(token_rows, dtype=jnp.int32), top_count)
    source = jnp.full((expert_count * capacity,), token_rows, jnp.int32).at[place].set(row_ids)
    return slots, source


def combine(table, expert_ids, slots, weights, zhi, rows_x, capacity):
    in_half = (expert_ids // rows_x) % 2 == zhi
    line = (expert_ids // (2 * rows_x)) * rows_x + expert_ids % rows_x
    blank = table.shape[0]
    index = jnp.where(in_half, line * capacity + slots, blank)
    padded = jnp.concatenate([table, jnp.zeros((1, table.shape[1]), table.dtype)], axis=0)
    chosen = padded[index.reshape(-1)].reshape(index.shape + (table.shape[1],))
    return jnp.sum(chosen.astype(jnp.float32) * weights[:, :, None], axis=1)


def run_layer(tokens, expert_ids, route_weights, gate_up, down, swap_in):
    rows_y, rows_x = lax.axis_size("y"), lax.axis_size("x")
    lines = rows_y * rows_x
    expert_count = 2 * lines
    chunks = lax.axis_size("zlo")
    token_rows, model_width = tokens.shape
    top_count = expert_ids.shape[1]
    capacity = min(token_rows, 3 * token_rows * top_count // (2 * expert_count))
    half_width = model_width // 2
    side = lax.axis_index("core")
    zhi = lax.axis_index("zhi")
    own_half = lax.dynamic_slice_in_dim(tokens, side * half_width, half_width, 1)
    mirror = [(high * chunks + low, (1 - high) * chunks + chunks - 1 - low) for high in range(2) for low in range(chunks)]
    far_half, far_ids, far_weights = lax.ppermute((own_half, expert_ids, route_weights), ("zhi", "zlo"), mirror)
    own_slots, own_source = routing(expert_ids, expert_count, capacity)
    far_slots, far_source = routing(far_ids, expert_count, capacity)

    def dispatch(rows, source):
        near = lax.dynamic_index_in_dim(source.reshape(rows_y, 2, rows_x, capacity), zhi, 1, keepdims=False)
        padded = jnp.concatenate([rows, jnp.zeros((1, half_width), rows.dtype)], axis=0)
        sent = padded[near.reshape(-1)].reshape(lines, capacity, half_width)
        return lax.all_to_all(sent, ("y", "x"), 0, 0, tiled=True)

    arrived = jnp.stack([dispatch(own_half, own_source), dispatch(far_half, far_source)], axis=0)
    total_rows = lines * 2 * capacity
    half_rows = total_rows // 2
    partial_value = jnp.dot(arrived.reshape(total_rows, half_width), gate_up, preferred_element_type=jnp.float32)
    mine = lax.dynamic_slice_in_dim(partial_value, side * half_rows, half_rows, 0)
    other = lax.dynamic_slice_in_dim(partial_value, (1 - side) * half_rows, half_rows, 0)
    summed = mine + lax.ppermute(other, "core", FLIP)
    block_units = gate_up.shape[1] // 2
    hidden = (jax.nn.silu(summed[:, :block_units]) * summed[:, block_units:]).astype(jnp.bfloat16)
    hidden, swap_in = lax.optimization_barrier((hidden, swap_in))
    swapped = swap_panels(*swap_in)
    gathered = lax.all_gather(hidden, "zlo", axis=0, tiled=False)
    gathered, swapped = lax.optimization_barrier((gathered, swapped))
    partner_part = lax.ppermute(gathered, "core", FLIP)
    keep_first = side == 0
    first_hidden = jnp.where(keep_first, gathered, partner_part)
    second_hidden = jnp.where(keep_first, partner_part, gathered)
    out_columns = down.shape[1]
    down_blocks = down.reshape(chunks, block_units, out_columns)

    def project(hidden_part):
        value = jnp.einsum("qrk,qkc->rc", hidden_part, down_blocks, preferred_element_type=jnp.float32)
        return value.astype(jnp.bfloat16)

    expert_out = jnp.concatenate([project(first_hidden), project(second_hidden)], axis=0)
    by_line = jnp.transpose(expert_out.reshape(2, lines, capacity, out_columns), (1, 0, 2, 3))
    returned = lax.all_to_all(by_line, ("y", "x"), 0, 0, tiled=True)
    own_table = returned[:, 0].reshape(lines * capacity, out_columns)
    far_table = returned[:, 1].reshape(lines * capacity, out_columns)
    far_sum = combine(far_table, far_ids, far_slots, far_weights, zhi, rows_x, capacity)
    own_sum = combine(own_table, expert_ids, own_slots, route_weights, zhi, rows_x, capacity)
    mixed = own_sum + lax.ppermute(far_sum, "zhi", FLIP)
    return mixed.astype(jnp.bfloat16), swapped


def per_device(tokens, expert_ids, route_weights, gate_up_panels, down_panels, partner):
    moe_out, (new_gate_up, new_down) = run_layer(
        tokens, expert_ids, route_weights, gate_up_panels[0, 0], down_panels[0],
        (gate_up_panels, down_panels, partner),
    )
    return (moe_out, new_gate_up, new_down)


def solution(mesh):
    experts, dps = mesh.devices.shape
    layout = mesh.devices.reshape(experts // 8, 2, 4, dps // 2, 2)
    split = Mesh(layout, EXPERT + DP)
    return jax.shard_map(
        per_device,
        mesh=split,
        in_specs=(
            P(EXPERT, None),
            P(EXPERT, None),
            P(EXPERT, None),
            P(EXPERT, DP, None, None),
            P(EXPERT, None, DP),
            P(),
        ),
        out_specs=(P(EXPERT, DP), P(EXPERT, DP, None, None), P(EXPERT, None, DP)),
        check_vma=False,
    )
```

```python
import jax
import jax.numpy as jnp
from jax import lax
from jax.sharding import Mesh
from jax.sharding import PartitionSpec as P

EXPERT = ("y", "zhi", "x")
DP = ("zlo", "core")
FLIP = [(0, 1), (1, 0)]


def swap_panels(gate_up, down, partner):
    here = lax.axis_index(EXPERT)
    kind = jnp.bitwise_xor(partner[here], here)
    even = (lax.axis_index("x") & 1) == 0
    gate_rows = gate_up.shape[2] // 2
    down_rows = down.shape[1] // 2
    lanes = gate_up.shape[3]
    down_shape = (down.shape[0], down_rows, down.shape[2])

    def pack(gate_part, down_part):
        return jnp.concatenate([gate_part[0, 0], down_part.reshape(-1, lanes)], axis=0)

    first = pack(gate_up[:, :, :gate_rows], down[:, :down_rows])
    second = pack(gate_up[:, :, gate_rows:], down[:, down_rows:])
    ring = lax.axis_size("x")
    ahead = [(i, (i + 1) % ring) for i in range(ring)]
    behind = [(i, (i + ring - 1) % ring) for i in range(ring)]
    from_behind = lax.ppermute(first, "x", ahead)
    from_ahead = lax.ppermute(second, "x", behind)
    is_two = kind == 2
    send_ahead = jnp.where(is_two, from_behind, second)
    send_behind = jnp.where(is_two, from_ahead, first)
    got_behind = lax.ppermute(send_ahead, "x", ahead)
    got_ahead = lax.ppermute(send_behind, "x", behind)
    one_even = (kind == 1) & even
    one_odd = (kind == 1) & ~even
    new_first = jnp.where(is_two, got_behind, jnp.where(one_even, got_ahead, jnp.where(one_odd, from_behind, first)))
    new_second = jnp.where(is_two, got_ahead, jnp.where(one_even, from_ahead, jnp.where(one_odd, got_behind, second)))
    new_gate_up = jnp.concatenate([new_first[:gate_rows], new_second[:gate_rows]], axis=0)[None, None]
    new_down = jnp.concatenate(
        [new_first[gate_rows:].reshape(down_shape), new_second[gate_rows:].reshape(down_shape)], axis=1
    )
    return (new_gate_up, new_down)


def routing(expert_ids, expert_count, capacity):
    token_rows, top_count = expert_ids.shape
    labels = jnp.arange(expert_count, dtype=jnp.int32)
    onehot = (expert_ids[:, :, None] == labels[None, None, :]).astype(jnp.int32)
    picked = jnp.sum(onehot, axis=1)
    slot_rank = jnp.cumsum(picked, axis=0) - picked
    slots = jnp.sum(onehot * slot_rank[:, None, :], axis=2)
    place = (expert_ids * capacity + slots).reshape(-1)
    row_ids = jnp.repeat(jnp.arange(token_rows, dtype=jnp.int32), top_count)
    source = jnp.full((expert_count * capacity,), token_rows, jnp.int32).at[place].set(row_ids)
    return slots, source


def combine(table, expert_ids, slots, weights, zhi, rows_x, capacity):
    in_half = (expert_ids // rows_x) % 2 == zhi
    line = (expert_ids // (2 * rows_x)) * rows_x + expert_ids % rows_x
    blank = table.shape[0]
    index = jnp.where(in_half, line * capacity + slots, blank)
    padded = jnp.concatenate([table, jnp.zeros((1, table.shape[1]), table.dtype)], axis=0)
    chosen = padded[index.reshape(-1)].reshape(index.shape + (table.shape[1],))
    return jnp.sum(chosen.astype(jnp.float32) * weights[:, :, None], axis=1)


def run_layer(tokens, expert_ids, route_weights, gate_up, down, swap_in):
    rows_y, rows_x = lax.axis_size("y"), lax.axis_size("x")
    lines = rows_y * rows_x
    expert_count = 2 * lines
    chunks = lax.axis_size("zlo")
    token_rows, model_width = tokens.shape
    top_count = expert_ids.shape[1]
    capacity = min(token_rows, 3 * token_rows * top_count // (2 * expert_count))
    half_width = model_width // 2
    side = lax.axis_index("core")
    zhi = lax.axis_index("zhi")
    own_half = lax.dynamic_slice_in_dim(tokens, side * half_width, half_width, 1)
    mirror = [(high * chunks + low, (1 - high) * chunks + chunks - 1 - low) for high in range(2) for low in range(chunks)]
    far_half, far_ids, far_weights = lax.ppermute((own_half, expert_ids, route_weights), ("zhi", "zlo"), mirror)
    own_slots, own_source = routing(expert_ids, expert_count, capacity)
    far_slots, far_source = routing(far_ids, expert_count, capacity)

    def dispatch(rows, source):
        near = lax.dynamic_index_in_dim(source.reshape(rows_y, 2, rows_x, capacity), zhi, 1, keepdims=False)
        pick = (near.reshape(-1, 1) == jnp.arange(token_rows, dtype=jnp.int32)[None, :]).astype(rows.dtype)
        sent = jnp.dot(pick, rows, preferred_element_type=jnp.float32).astype(rows.dtype)
        return lax.all_to_all(sent.reshape(lines, capacity, half_width), ("y", "x"), 0, 0, tiled=True)

    arrived = jnp.stack([dispatch(own_half, own_source), dispatch(far_half, far_source)], axis=0)
    total_rows = lines * 2 * capacity
    half_rows = total_rows // 2
    partial_value = jnp.dot(arrived.reshape(total_rows, half_width), gate_up, preferred_element_type=jnp.float32)
    mine = lax.dynamic_slice_in_dim(partial_value, side * half_rows, half_rows, 0)
    other = lax.dynamic_slice_in_dim(partial_value, (1 - side) * half_rows, half_rows, 0)
    summed = mine + lax.ppermute(other, "core", FLIP)
    block_units = gate_up.shape[1] // 2
    hidden = (jax.nn.silu(summed[:, :block_units]) * summed[:, block_units:]).astype(jnp.bfloat16)
    hidden, swap_in = lax.optimization_barrier((hidden, swap_in))
    swapped = swap_panels(*swap_in)
    gathered = lax.all_gather(hidden, "zlo", axis=0, tiled=False)
    gathered, swapped = lax.optimization_barrier((gathered, swapped))
    partner_part = lax.ppermute(gathered, "core", FLIP)
    keep_first = side == 0
    first_hidden = jnp.where(keep_first, gathered, partner_part)
    second_hidden = jnp.where(keep_first, partner_part, gathered)
    out_columns = down.shape[1]
    down_blocks = down.reshape(chunks, block_units, out_columns)

    def project(hidden_part):
        value = jnp.einsum("qrk,qkc->rc", hidden_part, down_blocks, preferred_element_type=jnp.float32)
        return value.astype(jnp.bfloat16)

    expert_out = jnp.concatenate([project(first_hidden), project(second_hidden)], axis=0)
    by_line = jnp.transpose(expert_out.reshape(2, lines, capacity, out_columns), (1, 0, 2, 3))
    returned = lax.all_to_all(by_line, ("y", "x"), 0, 0, tiled=True)
    own_table = returned[:, 0].reshape(lines * capacity, out_columns)
    far_table = returned[:, 1].reshape(lines * capacity, out_columns)
    far_sum = combine(far_table, far_ids, far_slots, far_weights, zhi, rows_x, capacity)
    own_sum = combine(own_table, expert_ids, own_slots, route_weights, zhi, rows_x, capacity)
    mixed = own_sum + lax.ppermute(far_sum, "zhi", FLIP)
    return mixed.astype(jnp.bfloat16), swapped


def per_device(tokens, expert_ids, route_weights, gate_up_panels, down_panels, partner):
    moe_out, (new_gate_up, new_down) = run_layer(
        tokens, expert_ids, route_weights, gate_up_panels[0, 0], down_panels[0],
        (gate_up_panels, down_panels, partner),
    )
    return (moe_out, new_gate_up, new_down)


def solution(mesh):
    experts, dps = mesh.devices.shape
    layout = mesh.devices.reshape(experts // 8, 2, 4, dps // 2, 2)
    split = Mesh(layout, EXPERT + DP)
    return jax.shard_map(
        per_device,
        mesh=split,
        in_specs=(
            P(EXPERT, None),
            P(EXPERT, None),
            P(EXPERT, None),
            P(EXPERT, DP, None, None),
            P(EXPERT, None, DP),
            P(),
        ),
        out_specs=(P(EXPERT, DP), P(EXPERT, DP, None, None), P(EXPERT, None, DP)),
        check_vma=False,
    )
```

```python
import jax
import jax.numpy as jnp
from jax import lax
from jax.sharding import Mesh
from jax.sharding import PartitionSpec as P

EXPERT = ("y", "zhi", "x")
DP = ("zlo", "core")
FLIP = [(0, 1), (1, 0)]


def swap_panels(gate_up, down, partner):
    here = lax.axis_index(EXPERT)
    kind = jnp.bitwise_xor(partner[here], here)
    even = (lax.axis_index("x") & 1) == 0
    gate_rows = gate_up.shape[2] // 2
    down_rows = down.shape[1] // 2
    first = (gate_up[:, :, :gate_rows], down[:, :down_rows])
    second = (gate_up[:, :, gate_rows:], down[:, down_rows:])
    ring = lax.axis_size("x")
    ahead = [(i, (i + 1) % ring) for i in range(ring)]
    behind = [(i, (i + ring - 1) % ring) for i in range(ring)]
    from_behind = lax.ppermute(first, "x", ahead)
    from_ahead = lax.ppermute(second, "x", behind)
    is_two = kind == 2

    def pick(flag, left, right):
        return tuple(jnp.where(flag, l, r) for l, r in zip(left, right))

    send_ahead = pick(is_two, from_behind, second)
    send_behind = pick(is_two, from_ahead, first)
    got_behind = lax.ppermute(send_ahead, "x", ahead)
    got_ahead = lax.ppermute(send_behind, "x", behind)
    one_even = (kind == 1) & even
    one_odd = (kind == 1) & ~even
    new_first = pick(is_two, got_behind, pick(one_even, got_ahead, pick(one_odd, from_behind, first)))
    new_second = pick(is_two, got_ahead, pick(one_even, from_ahead, pick(one_odd, got_behind, second)))
    new_gate_up = jnp.concatenate([new_first[0], new_second[0]], axis=2)
    new_down = jnp.concatenate([new_first[1], new_second[1]], axis=1)
    return (new_gate_up, new_down)


def routing(expert_ids, expert_count, capacity):
    token_rows, top_count = expert_ids.shape
    labels = jnp.arange(expert_count, dtype=jnp.int32)
    onehot = (expert_ids[:, :, None] == labels[None, None, :]).astype(jnp.int32)
    picked = jnp.sum(onehot, axis=1)
    slot_rank = jnp.cumsum(picked, axis=0) - picked
    slots = jnp.sum(onehot * slot_rank[:, None, :], axis=2)
    place = (expert_ids * capacity + slots).reshape(-1)
    row_ids = jnp.repeat(jnp.arange(token_rows, dtype=jnp.int32), top_count)
    source = jnp.full((expert_count * capacity,), token_rows, jnp.int32).at[place].set(row_ids)
    return slots, source


def combine(table, expert_ids, slots, weights, zhi, rows_x, capacity):
    in_half = (expert_ids // rows_x) % 2 == zhi
    line = (expert_ids // (2 * rows_x)) * rows_x + expert_ids % rows_x
    blank = table.shape[0]
    index = jnp.where(in_half, line * capacity + slots, blank)
    padded = jnp.concatenate([table, jnp.zeros((1, table.shape[1]), table.dtype)], axis=0)
    chosen = padded[index.reshape(-1)].reshape(index.shape + (table.shape[1],))
    return jnp.sum(chosen.astype(jnp.float32) * weights[:, :, None], axis=1)


def run_layer(tokens, expert_ids, route_weights, gate_up, down, swap_in):
    rows_y, rows_x = lax.axis_size("y"), lax.axis_size("x")
    lines = rows_y * rows_x
    expert_count = 2 * lines
    chunks = lax.axis_size("zlo")
    token_rows, model_width = tokens.shape
    top_count = expert_ids.shape[1]
    capacity = min(token_rows, 3 * token_rows * top_count // (2 * expert_count))
    half_width = model_width // 2
    side = lax.axis_index("core")
    zhi = lax.axis_index("zhi")
    own_half = lax.dynamic_slice_in_dim(tokens, side * half_width, half_width, 1)
    mirror = [(high * chunks + low, (1 - high) * chunks + chunks - 1 - low) for high in range(2) for low in range(chunks)]
    far_half, far_ids, far_weights = lax.ppermute((own_half, expert_ids, route_weights), ("zhi", "zlo"), mirror)
    own_slots, own_source = routing(expert_ids, expert_count, capacity)
    far_slots, far_source = routing(far_ids, expert_count, capacity)

    def dispatch(rows, source):
        near = lax.dynamic_index_in_dim(source.reshape(rows_y, 2, rows_x, capacity), zhi, 1, keepdims=False)
        pick = (near.reshape(-1, 1) == jnp.arange(token_rows, dtype=jnp.int32)[None, :]).astype(rows.dtype)
        sent = jnp.dot(pick, rows, preferred_element_type=jnp.float32).astype(rows.dtype)
        return lax.all_to_all(sent.reshape(lines, capacity, half_width), ("y", "x"), 0, 0, tiled=True)

    arrived = jnp.stack([dispatch(own_half, own_source), dispatch(far_half, far_source)], axis=0)
    total_rows = lines * 2 * capacity
    half_rows = total_rows // 2
    partial_value = jnp.dot(arrived.reshape(total_rows, half_width), gate_up, preferred_element_type=jnp.float32)
    mine = lax.dynamic_slice_in_dim(partial_value, side * half_rows, half_rows, 0)
    other = lax.dynamic_slice_in_dim(partial_value, (1 - side) * half_rows, half_rows, 0)
    summed = mine + lax.ppermute(other, "core", FLIP)
    block_units = gate_up.shape[1] // 2
    hidden = (jax.nn.silu(summed[:, :block_units]) * summed[:, block_units:]).astype(jnp.bfloat16)
    hidden, swap_in = lax.optimization_barrier((hidden, swap_in))
    swapped = swap_panels(*swap_in)
    gathered = lax.all_gather(hidden, "zlo", axis=0, tiled=False)
    gathered, swapped = lax.optimization_barrier((gathered, swapped))
    partner_part = lax.ppermute(gathered, "core", FLIP)
    keep_first = side == 0
    first_hidden = jnp.where(keep_first, gathered, partner_part)
    second_hidden = jnp.where(keep_first, partner_part, gathered)
    out_columns = down.shape[1]
    down_blocks = down.reshape(chunks, block_units, out_columns)

    def project(hidden_part):
        value = jnp.einsum("qrk,qkc->rc", hidden_part, down_blocks, preferred_element_type=jnp.float32)
        return value.astype(jnp.bfloat16)

    expert_out = jnp.concatenate([project(first_hidden), project(second_hidden)], axis=0)
    by_line = jnp.transpose(expert_out.reshape(2, lines, capacity, out_columns), (1, 0, 2, 3))
    returned = lax.all_to_all(by_line, ("y", "x"), 0, 0, tiled=True)
    own_table = returned[:, 0].reshape(lines * capacity, out_columns)
    far_table = returned[:, 1].reshape(lines * capacity, out_columns)
    far_sum = combine(far_table, far_ids, far_slots, far_weights, zhi, rows_x, capacity)
    own_sum = combine(own_table, expert_ids, own_slots, route_weights, zhi, rows_x, capacity)
    mixed = own_sum + lax.ppermute(far_sum, "zhi", FLIP)
    return mixed.astype(jnp.bfloat16), swapped


def per_device(tokens, expert_ids, route_weights, gate_up_panels, down_panels, partner):
    moe_out, (new_gate_up, new_down) = run_layer(
        tokens, expert_ids, route_weights, gate_up_panels[0, 0], down_panels[0],
        (gate_up_panels, down_panels, partner),
    )
    return (moe_out, new_gate_up, new_down)


def solution(mesh):
    experts, dps = mesh.devices.shape
    layout = mesh.devices.reshape(experts // 8, 2, 4, dps // 2, 2)
    split = Mesh(layout, EXPERT + DP)
    return jax.shard_map(
        per_device,
        mesh=split,
        in_specs=(
            P(EXPERT, None),
            P(EXPERT, None),
            P(EXPERT, None),
            P(EXPERT, DP, None, None),
            P(EXPERT, None, DP),
            P(),
        ),
        out_specs=(P(EXPERT, DP), P(EXPERT, DP, None, None), P(EXPERT, None, DP)),
        check_vma=False,
    )
```

```python
import jax
import jax.numpy as jnp
from jax import lax
from jax.sharding import Mesh
from jax.sharding import PartitionSpec as P

EXPERT = ("y", "zhi", "x")
DP = ("zlo", "core")
FLIP = [(0, 1), (1, 0)]


def swap_start(gate_up, down):
    gate_rows = gate_up.shape[2] // 2
    down_rows = down.shape[1] // 2
    first = (gate_up[:, :, :gate_rows], down[:, :down_rows])
    second = (gate_up[:, :, gate_rows:], down[:, down_rows:])
    ring = lax.axis_size("x")
    ahead = [(i, (i + 1) % ring) for i in range(ring)]
    behind = [(i, (i + ring - 1) % ring) for i in range(ring)]
    from_behind = lax.ppermute(first, "x", ahead)
    from_ahead = lax.ppermute(second, "x", behind)
    return (first, second, from_behind, from_ahead)


def swap_finish(state, partner):
    first, second, from_behind, from_ahead = state
    here = lax.axis_index(EXPERT)
    kind = jnp.bitwise_xor(partner[here], here)
    even = (lax.axis_index("x") & 1) == 0
    ring = lax.axis_size("x")
    ahead = [(i, (i + 1) % ring) for i in range(ring)]
    behind = [(i, (i + ring - 1) % ring) for i in range(ring)]
    is_two = kind == 2

    def pick(flag, left, right):
        return tuple(jnp.where(flag, l, r) for l, r in zip(left, right))

    send_ahead = pick(is_two, from_behind, second)
    send_behind = pick(is_two, from_ahead, first)
    got_behind = lax.ppermute(send_ahead, "x", ahead)
    got_ahead = lax.ppermute(send_behind, "x", behind)
    one_even = (kind == 1) & even
    one_odd = (kind == 1) & ~even
    new_first = pick(is_two, got_behind, pick(one_even, got_ahead, pick(one_odd, from_behind, first)))
    new_second = pick(is_two, got_ahead, pick(one_even, from_ahead, pick(one_odd, got_behind, second)))
    new_gate_up = jnp.concatenate([new_first[0], new_second[0]], axis=2)
    new_down = jnp.concatenate([new_first[1], new_second[1]], axis=1)
    return (new_gate_up, new_down)


def routing(expert_ids, expert_count, capacity):
    token_rows, top_count = expert_ids.shape
    labels = jnp.arange(expert_count, dtype=jnp.int32)
    onehot = (expert_ids[:, :, None] == labels[None, None, :]).astype(jnp.int32)
    picked = jnp.sum(onehot, axis=1)
    slot_rank = jnp.cumsum(picked, axis=0) - picked
    slots = jnp.sum(onehot * slot_rank[:, None, :], axis=2)
    place = (expert_ids * capacity + slots).reshape(-1)
    row_ids = jnp.repeat(jnp.arange(token_rows, dtype=jnp.int32), top_count)
    source = jnp.full((expert_count * capacity,), token_rows, jnp.int32).at[place].set(row_ids)
    return slots, source


def combine(table, expert_ids, slots, weights, zhi, rows_x, capacity):
    in_half = (expert_ids // rows_x) % 2 == zhi
    line = (expert_ids // (2 * rows_x)) * rows_x + expert_ids % rows_x
    blank = table.shape[0]
    index = jnp.where(in_half, line * capacity + slots, blank)
    padded = jnp.concatenate([table, jnp.zeros((1, table.shape[1]), table.dtype)], axis=0)
    chosen = padded[index.reshape(-1)].reshape(index.shape + (table.shape[1],))
    return jnp.sum(chosen.astype(jnp.float32) * weights[:, :, None], axis=1)


def run_layer(tokens, expert_ids, route_weights, gate_up, down, swap_in):
    rows_y, rows_x = lax.axis_size("y"), lax.axis_size("x")
    lines = rows_y * rows_x
    expert_count = 2 * lines
    chunks = lax.axis_size("zlo")
    token_rows, model_width = tokens.shape
    top_count = expert_ids.shape[1]
    capacity = min(token_rows, 3 * token_rows * top_count // (2 * expert_count))
    half_width = model_width // 2
    side = lax.axis_index("core")
    zhi = lax.axis_index("zhi")
    own_half = lax.dynamic_slice_in_dim(tokens, side * half_width, half_width, 1)
    mirror = [(high * chunks + low, (1 - high) * chunks + chunks - 1 - low) for high in range(2) for low in range(chunks)]
    swap_state = swap_start(swap_in[0], swap_in[1])
    far_half, far_ids, far_weights = lax.ppermute((own_half, expert_ids, route_weights), ("zhi", "zlo"), mirror)
    far_half, swap_state = lax.optimization_barrier((far_half, swap_state))
    own_slots, own_source = routing(expert_ids, expert_count, capacity)
    far_slots, far_source = routing(far_ids, expert_count, capacity)

    def dispatch(rows, source):
        near = lax.dynamic_index_in_dim(source.reshape(rows_y, 2, rows_x, capacity), zhi, 1, keepdims=False)
        pick = (near.reshape(-1, 1) == jnp.arange(token_rows, dtype=jnp.int32)[None, :]).astype(rows.dtype)
        sent = jnp.dot(pick, rows, preferred_element_type=jnp.float32).astype(rows.dtype)
        return lax.all_to_all(sent.reshape(lines, capacity, half_width), ("y", "x"), 0, 0, tiled=True)

    arrived = jnp.stack([dispatch(own_half, own_source), dispatch(far_half, far_source)], axis=0)
    total_rows = lines * 2 * capacity
    half_rows = total_rows // 2
    partial_value = jnp.dot(arrived.reshape(total_rows, half_width), gate_up, preferred_element_type=jnp.float32)
    mine = lax.dynamic_slice_in_dim(partial_value, side * half_rows, half_rows, 0)
    other = lax.dynamic_slice_in_dim(partial_value, (1 - side) * half_rows, half_rows, 0)
    summed = mine + lax.ppermute(other, "core", FLIP)
    block_units = gate_up.shape[1] // 2
    hidden = (jax.nn.silu(summed[:, :block_units]) * summed[:, block_units:]).astype(jnp.bfloat16)
    hidden, swap_state = lax.optimization_barrier((hidden, swap_state))
    swapped = swap_finish(swap_state, swap_in[2])
    gathered = lax.all_gather(hidden, "zlo", axis=0, tiled=False)
    gathered, swapped = lax.optimization_barrier((gathered, swapped))
    partner_part = lax.ppermute(gathered, "core", FLIP)
    keep_first = side == 0
    first_hidden = jnp.where(keep_first, gathered, partner_part)
    second_hidden = jnp.where(keep_first, partner_part, gathered)
    out_columns = down.shape[1]
    down_blocks = down.reshape(chunks, block_units, out_columns)

    def project(hidden_part):
        value = jnp.einsum("qrk,qkc->rc", hidden_part, down_blocks, preferred_element_type=jnp.float32)
        return value.astype(jnp.bfloat16)

    expert_out = jnp.concatenate([project(first_hidden), project(second_hidden)], axis=0)
    by_line = jnp.transpose(expert_out.reshape(2, lines, capacity, out_columns), (1, 0, 2, 3))
    returned = lax.all_to_all(by_line, ("y", "x"), 0, 0, tiled=True)
    own_table = returned[:, 0].reshape(lines * capacity, out_columns)
    far_table = returned[:, 1].reshape(lines * capacity, out_columns)
    far_sum = combine(far_table, far_ids, far_slots, far_weights, zhi, rows_x, capacity)
    own_sum = combine(own_table, expert_ids, own_slots, route_weights, zhi, rows_x, capacity)
    mixed = own_sum + lax.ppermute(far_sum, "zhi", FLIP)
    return mixed.astype(jnp.bfloat16), swapped


def per_device(tokens, expert_ids, route_weights, gate_up_panels, down_panels, partner):
    moe_out, (new_gate_up, new_down) = run_layer(
        tokens, expert_ids, route_weights, gate_up_panels[0, 0], down_panels[0],
        (gate_up_panels, down_panels, partner),
    )
    return (moe_out, new_gate_up, new_down)


def solution(mesh):
    experts, dps = mesh.devices.shape
    layout = mesh.devices.reshape(experts // 8, 2, 4, dps // 2, 2)
    split = Mesh(layout, EXPERT + DP)
    return jax.shard_map(
        per_device,
        mesh=split,
        in_specs=(
            P(EXPERT, None),
            P(EXPERT, None),
            P(EXPERT, None),
            P(EXPERT, DP, None, None),
            P(EXPERT, None, DP),
            P(),
        ),
        out_specs=(P(EXPERT, DP), P(EXPERT, DP, None, None), P(EXPERT, None, DP)),
        check_vma=False,
    )
```

```python
import jax
import jax.numpy as jnp
from jax import lax
from jax.sharding import Mesh
from jax.sharding import PartitionSpec as P

EXPERT = ("y", "zhi", "x")
DP = ("zlo", "core")
FLIP = [(0, 1), (1, 0)]


def swap_panels(gate_up, down, partner):
    here = lax.axis_index(EXPERT)
    kind = jnp.bitwise_xor(partner[here], here)
    even = (lax.axis_index("x") & 1) == 0
    gate_rows = gate_up.shape[2] // 2
    down_rows = down.shape[1] // 2
    first = (gate_up[:, :, :gate_rows], down[:, :down_rows])
    second = (gate_up[:, :, gate_rows:], down[:, down_rows:])
    ring = lax.axis_size("x")
    ahead = [(i, (i + 1) % ring) for i in range(ring)]
    behind = [(i, (i + ring - 1) % ring) for i in range(ring)]
    from_behind = lax.ppermute(first, "x", ahead)
    from_ahead = lax.ppermute(second, "x", behind)
    is_two = kind == 2

    def pick(flag, left, right):
        return tuple(jnp.where(flag, l, r) for l, r in zip(left, right))

    send_ahead = pick(is_two, from_behind, second)
    send_behind = pick(is_two, from_ahead, first)
    got_behind = lax.ppermute(send_ahead, "x", ahead)
    got_ahead = lax.ppermute(send_behind, "x", behind)
    one_even = (kind == 1) & even
    one_odd = (kind == 1) & ~even
    new_first = pick(is_two, got_behind, pick(one_even, got_ahead, pick(one_odd, from_behind, first)))
    new_second = pick(is_two, got_ahead, pick(one_even, from_ahead, pick(one_odd, got_behind, second)))
    new_gate_up = jnp.concatenate([new_first[0], new_second[0]], axis=2)
    new_down = jnp.concatenate([new_first[1], new_second[1]], axis=1)
    return (new_gate_up, new_down)


def routing(expert_ids, expert_count, capacity):
    token_rows, top_count = expert_ids.shape
    labels = jnp.arange(expert_count, dtype=jnp.int32)
    onehot = (expert_ids[:, :, None] == labels[None, None, :]).astype(jnp.int32)
    picked = jnp.sum(onehot, axis=1)
    slot_rank = jnp.cumsum(picked, axis=0) - picked
    slots = jnp.sum(onehot * slot_rank[:, None, :], axis=2)
    place = (expert_ids * capacity + slots).reshape(-1)
    row_ids = jnp.repeat(jnp.arange(token_rows, dtype=jnp.int32), top_count)
    source = jnp.full((expert_count * capacity,), token_rows, jnp.int32).at[place].set(row_ids)
    return slots, source


def combine(table, expert_ids, slots, weights, zhi, rows_x, capacity):
    in_half = (expert_ids // rows_x) % 2 == zhi
    line = (expert_ids // (2 * rows_x)) * rows_x + expert_ids % rows_x
    blank = table.shape[0]
    index = jnp.where(in_half, line * capacity + slots, blank)
    padded = jnp.concatenate([table, jnp.zeros((1, table.shape[1]), table.dtype)], axis=0)
    chosen = padded[index.reshape(-1)].reshape(index.shape + (table.shape[1],))
    return jnp.sum(chosen.astype(jnp.float32) * weights[:, :, None], axis=1)


def run_layer(tokens, expert_ids, route_weights, gate_up, down, swap_in):
    rows_y, rows_x = lax.axis_size("y"), lax.axis_size("x")
    lines = rows_y * rows_x
    expert_count = 2 * lines
    chunks = lax.axis_size("zlo")
    token_rows, model_width = tokens.shape
    top_count = expert_ids.shape[1]
    capacity = min(token_rows, 3 * token_rows * top_count // (2 * expert_count))
    half_width = model_width // 2
    side = lax.axis_index("core")
    zhi = lax.axis_index("zhi")
    own_half = lax.dynamic_slice_in_dim(tokens, side * half_width, half_width, 1)
    mirror = [(high * chunks + low, (1 - high) * chunks + chunks - 1 - low) for high in range(2) for low in range(chunks)]
    far_half, far_ids, far_weights = lax.ppermute((own_half, expert_ids, route_weights), ("zhi", "zlo"), mirror)
    own_slots, own_source = routing(expert_ids, expert_count, capacity)
    far_slots, far_source = routing(far_ids, expert_count, capacity)

    def dispatch(rows, source):
        near = lax.dynamic_index_in_dim(source.reshape(rows_y, 2, rows_x, capacity), zhi, 1, keepdims=False)
        pick = (near.reshape(-1, 1) == jnp.arange(token_rows, dtype=jnp.int32)[None, :]).astype(rows.dtype)
        sent = jnp.dot(pick, rows, preferred_element_type=jnp.float32).astype(rows.dtype)
        return lax.all_to_all(sent.reshape(lines, capacity, half_width), ("y", "x"), 0, 0, tiled=True)

    part_rows = lines * capacity

    def partial(arrived):
        return jnp.dot(arrived.reshape(part_rows, half_width), gate_up, preferred_element_type=jnp.float32)

    own_value = partial(dispatch(own_half, own_source))
    far_value = partial(dispatch(far_half, far_source))
    keep_own = side == 0
    mine = jnp.where(keep_own, own_value, far_value)
    other = jnp.where(keep_own, far_value, own_value)
    summed = mine + lax.ppermute(other, "core", FLIP)
    block_units = gate_up.shape[1] // 2
    hidden = (jax.nn.silu(summed[:, :block_units]) * summed[:, block_units:]).astype(jnp.bfloat16)
    hidden, swap_in = lax.optimization_barrier((hidden, swap_in))
    swapped = swap_panels(*swap_in)
    gathered = lax.all_gather(hidden, "zlo", axis=0, tiled=False)
    gathered, swapped = lax.optimization_barrier((gathered, swapped))
    partner_part = lax.ppermute(gathered, "core", FLIP)
    keep_first = side == 0
    first_hidden = jnp.where(keep_first, gathered, partner_part)
    second_hidden = jnp.where(keep_first, partner_part, gathered)
    out_columns = down.shape[1]
    down_blocks = down.reshape(chunks, block_units, out_columns)

    def project(hidden_part):
        value = jnp.einsum("qrk,qkc->rc", hidden_part, down_blocks, preferred_element_type=jnp.float32)
        return value.astype(jnp.bfloat16)

    expert_out = jnp.concatenate([project(first_hidden), project(second_hidden)], axis=0)
    by_line = jnp.transpose(expert_out.reshape(2, lines, capacity, out_columns), (1, 0, 2, 3))
    returned = lax.all_to_all(by_line, ("y", "x"), 0, 0, tiled=True)
    own_table = returned[:, 0].reshape(lines * capacity, out_columns)
    far_table = returned[:, 1].reshape(lines * capacity, out_columns)
    far_sum = combine(far_table, far_ids, far_slots, far_weights, zhi, rows_x, capacity)
    own_sum = combine(own_table, expert_ids, own_slots, route_weights, zhi, rows_x, capacity)
    mixed = own_sum + lax.ppermute(far_sum, "zhi", FLIP)
    return mixed.astype(jnp.bfloat16), swapped


def per_device(tokens, expert_ids, route_weights, gate_up_panels, down_panels, partner):
    moe_out, (new_gate_up, new_down) = run_layer(
        tokens, expert_ids, route_weights, gate_up_panels[0, 0], down_panels[0],
        (gate_up_panels, down_panels, partner),
    )
    return (moe_out, new_gate_up, new_down)


def solution(mesh):
    experts, dps = mesh.devices.shape
    layout = mesh.devices.reshape(experts // 8, 2, 4, dps // 2, 2)
    split = Mesh(layout, EXPERT + DP)
    return jax.shard_map(
        per_device,
        mesh=split,
        in_specs=(
            P(EXPERT, None),
            P(EXPERT, None),
            P(EXPERT, None),
            P(EXPERT, DP, None, None),
            P(EXPERT, None, DP),
            P(),
        ),
        out_specs=(P(EXPERT, DP), P(EXPERT, DP, None, None), P(EXPERT, None, DP)),
        check_vma=False,
    )
```

```python
import jax
import jax.numpy as jnp
from jax import lax
from jax.sharding import Mesh
from jax.sharding import PartitionSpec as P

EXPERT = ("y", "zhi", "x")
DP = ("zlo", "core")
FLIP = [(0, 1), (1, 0)]


def swap_panels(gate_up, down, partner):
    here = lax.axis_index(EXPERT)
    kind = jnp.bitwise_xor(partner[here], here)
    even = (lax.axis_index("x") & 1) == 0
    gate_rows = gate_up.shape[2] // 2
    down_rows = down.shape[1] // 2
    first = (gate_up[:, :, :gate_rows], down[:, :down_rows])
    second = (gate_up[:, :, gate_rows:], down[:, down_rows:])
    ring = lax.axis_size("x")
    ahead = [(i, (i + 1) % ring) for i in range(ring)]
    behind = [(i, (i + ring - 1) % ring) for i in range(ring)]
    from_behind = lax.ppermute(first, "x", ahead)
    from_ahead = lax.ppermute(second, "x", behind)
    is_two = kind == 2

    def pick(flag, left, right):
        return tuple(jnp.where(flag, l, r) for l, r in zip(left, right))

    send_ahead = pick(is_two, from_behind, second)
    send_behind = pick(is_two, from_ahead, first)
    got_behind = lax.ppermute(send_ahead, "x", ahead)
    got_ahead = lax.ppermute(send_behind, "x", behind)
    one_even = (kind == 1) & even
    one_odd = (kind == 1) & ~even
    new_first = pick(is_two, got_behind, pick(one_even, got_ahead, pick(one_odd, from_behind, first)))
    new_second = pick(is_two, got_ahead, pick(one_even, from_ahead, pick(one_odd, got_behind, second)))
    new_gate_up = jnp.concatenate([new_first[0], new_second[0]], axis=2)
    new_down = jnp.concatenate([new_first[1], new_second[1]], axis=1)
    return (new_gate_up, new_down)


def routing(expert_ids, expert_count, capacity):
    token_rows, top_count = expert_ids.shape
    labels = jnp.arange(expert_count, dtype=jnp.int32)
    onehot = (expert_ids[:, :, None] == labels[None, None, :]).astype(jnp.int32)
    picked = jnp.sum(onehot, axis=1)
    slot_rank = jnp.cumsum(picked, axis=0) - picked
    slots = jnp.sum(onehot * slot_rank[:, None, :], axis=2)
    place = (expert_ids * capacity + slots).reshape(-1)
    row_ids = jnp.repeat(jnp.arange(token_rows, dtype=jnp.int32), top_count)
    source = jnp.full((expert_count * capacity,), token_rows, jnp.int32).at[place].set(row_ids)
    return slots, source


def combine(table, expert_ids, slots, weights, zhi, rows_x, capacity):
    in_half = (expert_ids // rows_x) % 2 == zhi
    line = (expert_ids // (2 * rows_x)) * rows_x + expert_ids % rows_x
    blank = table.shape[0]
    index = jnp.where(in_half, line * capacity + slots, blank)
    padded = jnp.concatenate([table, jnp.zeros((1, table.shape[1]), table.dtype)], axis=0)
    chosen = padded[index.reshape(-1)].reshape(index.shape + (table.shape[1],))
    return jnp.sum(chosen.astype(jnp.float32) * weights[:, :, None], axis=1)


def run_layer(tokens, expert_ids, route_weights, gate_up, down, swap_in):
    rows_y, rows_x = lax.axis_size("y"), lax.axis_size("x")
    lines = rows_y * rows_x
    expert_count = 2 * lines
    chunks = lax.axis_size("zlo")
    token_rows, model_width = tokens.shape
    top_count = expert_ids.shape[1]
    capacity = min(token_rows, 3 * token_rows * top_count // (2 * expert_count))
    half_width = model_width // 2
    side = lax.axis_index("core")
    zhi = lax.axis_index("zhi")
    own_half = lax.dynamic_slice_in_dim(tokens, side * half_width, half_width, 1)
    mirror = [(high * chunks + low, (1 - high) * chunks + chunks - 1 - low) for high in range(2) for low in range(chunks)]
    far_half, far_ids, far_weights = lax.ppermute((own_half, expert_ids, route_weights), ("zhi", "zlo"), mirror)
    own_slots, own_source = routing(expert_ids, expert_count, capacity)
    far_slots, far_source = routing(far_ids, expert_count, capacity)

    def dispatch(rows, source):
        near = lax.dynamic_index_in_dim(source.reshape(rows_y, 2, rows_x, capacity), zhi, 1, keepdims=False)
        pick = (near.reshape(-1, 1) == jnp.arange(token_rows, dtype=jnp.int32)[None, :]).astype(rows.dtype)
        sent = jnp.dot(pick, rows, preferred_element_type=jnp.float32).astype(rows.dtype)
        return lax.all_to_all(sent.reshape(lines, capacity, half_width), ("y", "x"), 0, 0, tiled=True)

    part_rows = lines * capacity

    def partial(arrived):
        return jnp.dot(arrived.reshape(part_rows, half_width), gate_up, preferred_element_type=jnp.float32)

    own_value = partial(dispatch(own_half, own_source))
    far_value = partial(dispatch(far_half, far_source))
    keep_own = side == 0
    mine = jnp.where(keep_own, own_value, far_value)
    other = jnp.where(keep_own, far_value, own_value)
    summed = mine + lax.ppermute(other, "core", FLIP)
    block_units = gate_up.shape[1] // 2
    hidden = (jax.nn.silu(summed[:, :block_units]) * summed[:, block_units:]).astype(jnp.bfloat16)
    hidden, swap_in = lax.optimization_barrier((hidden, swap_in))
    swapped = swap_panels(*swap_in)
    gathered = lax.all_gather(hidden, "zlo", axis=0, tiled=False)
    gathered, swapped = lax.optimization_barrier((gathered, swapped))
    partner_part = lax.ppermute(gathered, "core", FLIP)
    keep_first = side == 0
    first_hidden = jnp.where(keep_first, gathered, partner_part)
    second_hidden = jnp.where(keep_first, partner_part, gathered)
    out_columns = down.shape[1]
    down_blocks = down.reshape(chunks, block_units, out_columns)

    def project(hidden_part):
        value = jnp.einsum("qrk,qkc->rc", hidden_part, down_blocks, preferred_element_type=jnp.float32)
        return value.astype(jnp.bfloat16)

    by_line = jnp.stack(
        [project(part).reshape(lines, capacity, out_columns) for part in (first_hidden, second_hidden)], axis=1
    )
    returned = lax.all_to_all(by_line, ("y", "x"), 0, 0, tiled=True)
    own_table = returned[:, 0].reshape(lines * capacity, out_columns)
    far_table = returned[:, 1].reshape(lines * capacity, out_columns)
    far_sum = combine(far_table, far_ids, far_slots, far_weights, zhi, rows_x, capacity)
    own_sum = combine(own_table, expert_ids, own_slots, route_weights, zhi, rows_x, capacity)
    mixed = own_sum + lax.ppermute(far_sum, "zhi", FLIP)
    return mixed.astype(jnp.bfloat16), swapped


def per_device(tokens, expert_ids, route_weights, gate_up_panels, down_panels, partner):
    moe_out, (new_gate_up, new_down) = run_layer(
        tokens, expert_ids, route_weights, gate_up_panels[0, 0], down_panels[0],
        (gate_up_panels, down_panels, partner),
    )
    return (moe_out, new_gate_up, new_down)


def solution(mesh):
    experts, dps = mesh.devices.shape
    layout = mesh.devices.reshape(experts // 8, 2, 4, dps // 2, 2)
    split = Mesh(layout, EXPERT + DP)
    return jax.shard_map(
        per_device,
        mesh=split,
        in_specs=(
            P(EXPERT, None),
            P(EXPERT, None),
            P(EXPERT, None),
            P(EXPERT, DP, None, None),
            P(EXPERT, None, DP),
            P(),
        ),
        out_specs=(P(EXPERT, DP), P(EXPERT, DP, None, None), P(EXPERT, None, DP)),
        check_vma=False,
    )
```
